256 devices in a mesh: gx: 8 (over y, core), gy: 32 (over x, z).
Axes of the slice: x: 4, y: 4, z: 8, core: 2. Of those that a mesh axis runs over, the one named last changes fastest.
Arguments:
- inputs: bfloat16 [3072, 7168], P('gy', 'gx'), may hold values from -6 to 6
- query_weight: bfloat16 [7168, 7168], P('gy', 'gx'), may hold values from -0.0625 to 0.0625
- key_weight: bfloat16 [7168, 7168], P('gy', 'gx'), may hold values from -0.0625 to 0.0625
- value_weight: bfloat16 [7168, 7168], P('gy', 'gx'), may hold values from -0.0625 to 0.0625
- adapter_down: bfloat16 [128, 7168], P(None, 'gx'), may hold values from -0.0625 to 0.0625
- adapter_up: bfloat16 [7168, 128], P('gy'), may hold values from -0.5 to 0.5
- prompt_keys: bfloat16 [8, 7168, 2048], P('gx', 'gy'), may hold values from -6 to 6
- prompt_values: bfloat16 [8, 7168, 2048], P('gx', 'gy'), may hold values from -6 to 6
- cache_keys: bfloat16 [64, 7168, 512], P('gx', 'gy'), may hold values from -240 to 240
- cache_values: bfloat16 [64, 7168, 512], P('gx', 'gy'), may hold values from -6 to 6
- cache_lengths: int32 [64], P('gx'), may hold values from 1 to 512, as said below
- parents: int32 [64, 48], P('gx'), may hold values from 0 to 46, as said below
- out_weight: bfloat16 [7168, 3584], P('gy', 'gx'), may hold values from -0.125 to 0.125
Outputs:
- layer_output: bfloat16 [3072, 3584], P('gx', 'gy')
The draws below stay inside these ranges and needn't reach their ends.
Inputs may be any that keep to these rules, and one draw needn't show every extreme that they name: `parents`: node n's parent is a node below n, node 0 is its own parent, and node 47 hangs from node 46. `cache_lengths`: some request has all 512 positions valid.
All inputs are finite; a program needn't handle non-finite values.
Results may differ from the reference program's by a relative error of at most 0.017.
Values may be sent and summed in bfloat16 or wider, within the bound.
No kernel may reach another device: no remote copies, remote signals or barrier semaphores. Data moves between devices by JAX's collectives and lax.ppermute only.
A program may use at most 128 MiB of HBM per device.

```python
import math
import jax
import jax.numpy as jnp
from jax import lax

DIN = 7168
DM = 3584
HEAD = 224
RANK = 128
NODES = 48
REQ_DEV = 8
PROMPT = 2048
CACHE = 512
HEADS = 32
HD = 7168
GROUPS = 8
REQ = 64
TOKENS = 3072


def draw_parents(key, part):
    columns = jnp.arange(NODES, dtype=jnp.int32)
    ceiling = jnp.maximum(columns, 1)
    drawn = jax.random.randint(key, (REQ, NODES), 0, 1 << 20, dtype=jnp.int32)
    chosen = drawn % ceiling[None, :]
    return jnp.where(columns[None, :] == NODES - 1, NODES - 2, chosen).astype(jnp.int32)


def draw_cache_lengths(key, part):
    drawn = jax.random.randint(key, (REQ,), 1, CACHE + 1, dtype=jnp.int32)
    fullest = jax.random.randint(jax.random.fold_in(key, 7), (), 0, REQ, dtype=jnp.int32)
    return jnp.where(jnp.arange(REQ, dtype=jnp.int32) == fullest, CACHE, drawn).astype(jnp.int32)


def draw_cache_keys(key, part):
    values = jnp.clip(jax.random.normal(key, (REQ, HD, CACHE), jnp.float32), -6.0, 6.0)
    return values.astype(jnp.bfloat16)


def raised(entries, stream_key, source, target, shards_of, factor):
    def block_of(axis_at):
        return (jnp.arange(entries.shape[axis_at]) // (entries.shape[axis_at] // shards_of)).reshape((-1,) + (1,) * (entries.ndim - 1 - axis_at))

    first = jax.random.permutation(stream_key, shards_of)[block_of(target)]
    far = (block_of(target) + shards_of // 2) % shards_of
    return jnp.where((block_of(source) == first) | (block_of(source) == far), factor * entries, entries)


def shard_levels(rng, extent, shards, least, high):
    factor_of = 1.0
    for position, shards_of in shards:
        heights = jax.random.uniform(jax.random.fold_in(jax.random.fold_in(rng, 6), position), (shards_of,), jnp.float32, least / len(shards), high / len(shards))
        factor_of = factor_of * jnp.repeat(jnp.exp(heights), extent[position] // shards_of).reshape((-1,) + (1,) * (len(extent) - 1 - position))
    return factor_of


def noise(own_key, shape, scale, reach, shards=(), held_as=jnp.bfloat16):
    values = jax.random.normal(own_key, shape, jnp.float32) * scale
    if len(shards) > 0:
        values = shard_levels(own_key, shape, shards, -0.22, 0.18) * values
    return jnp.clip(values, min=-reach, max=reach).astype(held_as)


def gaussian_with(stream_key, extent, scale, most, cuts, heavy, held_as=jnp.bfloat16):
    values = scale * jax.random.normal(stream_key, extent, jnp.float32)
    if cuts:
        values = values * shard_levels(stream_key, extent, cuts, -0.22, 0.18)
    return jnp.clip(raised(values, jax.random.fold_in(stream_key, 3), *heavy), -most, most).astype(held_as)


def setup_inputs(seed: int = 0) -> dict:
    streams_of = jax.random.split(jax.random.key(seed), 14)
    return {
        "inputs": noise(streams_of[0], (TOKENS, DIN), 1.0, 6.0, ((0, 32), (1, 8))),
        "query_weight": noise(streams_of[1], (HD, DIN), DIN ** -0.5, 0.0625, ((0, 32), (1, 8))),
        "key_weight": noise(streams_of[2], (HD, DIN), DIN ** -0.5, 0.0625, ((0, 32), (1, 8))),
        "value_weight": noise(streams_of[3], (HD, DIN), DIN ** -0.5, 0.0625, ((0, 32), (1, 8))),
        "adapter_down": noise(streams_of[4], (RANK, DIN), DIN ** -0.5, 0.0625, ((1, 8),)),
        "adapter_up": noise(streams_of[5], (HD, RANK), RANK ** -0.5, 0.5, ((0, 32),)),
        "prompt_keys": noise(streams_of[6], (GROUPS, HD, PROMPT), 1.0, 6.0, ((0, 8), (1, 32))),
        "prompt_values": noise(streams_of[7], (GROUPS, HD, PROMPT), 1.0, 6.0, ((0, 8), (1, 32))),
        "cache_keys": draw_cache_keys(jax.random.fold_in(streams_of[13], 71), 0),
        "cache_values": noise(streams_of[9], (REQ, HD, CACHE), 1.0, 6.0, ((0, 8), (1, 32))),
        "cache_lengths": draw_cache_lengths(jax.random.fold_in(streams_of[13], 71), 0),
        "parents": draw_parents(jax.random.fold_in(streams_of[13], 71), 0),
        "out_weight": gaussian_with(streams_of[12], (HD, DM), HD ** -0.5, 0.125, ((0, 32), (1, 8)), (0, 1, 32, 2.75)),
    }


def ancestors(parents):
    node_count = parents.shape[1]
    columns = jnp.arange(node_count, dtype=jnp.int32)
    parent_hot = (parents[:, :, None] == columns[None, None, :]).astype(jnp.float32)
    reached = jnp.minimum(jnp.eye(node_count, dtype=jnp.float32)[None] + parent_hot, 1.0)
    rounds = max(1, math.ceil(math.log2(node_count)))
    for sweep in range(rounds):
        reached = jnp.minimum(reached + jnp.einsum('rnm,rmk->rnk', reached, reached, precision=lax.Precision.HIGHEST), 1.0)
    return reached

def attend(queries, new_keys, new_values, prompt_k, prompt_v, cache_k, cache_v, lengths, parents):
    factor = 1.0 / math.sqrt(queries.shape[-1])
    query_f = queries.astype(jnp.float32)
    s_prompt = jnp.einsum('rnhe,hep->rnhp', query_f, prompt_k.astype(jnp.float32)) * factor
    s_cache = jnp.einsum('rnhe,rhec->rnhc', query_f, cache_k.astype(jnp.float32)) * factor
    s_tree = jnp.einsum('rnhe,rmhe->rnhm', query_f, new_keys.astype(jnp.float32)) * factor
    usable = jnp.arange(cache_k.shape[-1], dtype=jnp.int32)[None, :] < lengths[:, None]
    s_cache = jnp.where(usable[:, None, None, :], s_cache, -jnp.inf)
    reached = ancestors(parents)
    s_tree = jnp.where(reached[:, :, None, :] > 0.5, s_tree, -jnp.inf)
    largest = jnp.maximum(jnp.maximum(lax.optimization_barrier(jnp.max(s_prompt, axis=-1, keepdims=True)), lax.optimization_barrier(jnp.max(s_cache, axis=-1, keepdims=True))), lax.optimization_barrier(jnp.max(s_tree, axis=-1, keepdims=True)))
    e_prompt = jnp.exp(s_prompt - largest)
    e_cache = jnp.exp(s_cache - largest)
    e_tree = jnp.exp(s_tree - largest)
    totals = lax.optimization_barrier(jnp.sum(e_prompt, axis=-1, keepdims=True)) + lax.optimization_barrier(jnp.sum(e_cache, axis=-1, keepdims=True)) + lax.optimization_barrier(jnp.sum(e_tree, axis=-1, keepdims=True))
    w_prompt = (e_prompt / totals).astype(jnp.bfloat16).astype(jnp.float32)
    w_cache = (e_cache / totals).astype(jnp.bfloat16).astype(jnp.float32)
    w_tree = (e_tree / totals).astype(jnp.bfloat16).astype(jnp.float32)
    result = jnp.einsum('rnhp,hep->rnhe', w_prompt, prompt_v.astype(jnp.float32))
    result = result + jnp.einsum('rnhc,rhec->rnhe', w_cache, cache_v.astype(jnp.float32))
    result = result + jnp.einsum('rnhm,rmhe->rnhe', w_tree, new_values.astype(jnp.float32))
    return result.astype(jnp.bfloat16)

def reference(inputs, query_weight, key_weight, value_weight, adapter_down, adapter_up, prompt_keys, prompt_values, cache_keys, cache_values, cache_lengths, parents, out_weight):
    query_base = jnp.dot(inputs, query_weight.T, preferred_element_type=jnp.float32)
    new_keys = jnp.dot(inputs, key_weight.T, preferred_element_type=jnp.float32).astype(jnp.bfloat16)
    new_values = jnp.dot(inputs, value_weight.T, preferred_element_type=jnp.float32).astype(jnp.bfloat16)
    adapter_mid = jnp.dot(inputs, adapter_down.T, preferred_element_type=jnp.float32).astype(jnp.bfloat16)
    queries = (query_base + jnp.dot(adapter_mid, adapter_up.T, preferred_element_type=jnp.float32)).astype(jnp.bfloat16)
    shaped = (GROUPS, REQ_DEV, NODES, HEADS, HEAD)
    cached = (GROUPS, REQ_DEV, HEADS, HEAD, CACHE)
    prompted = (GROUPS, HEADS, HEAD, PROMPT)

    def one_group(operands):
        return attend(operands[0], operands[1], operands[2], operands[3], operands[4], operands[5], operands[6], operands[7], operands[8])
    attended = lax.map(one_group, (queries.reshape(shaped), new_keys.reshape(shaped), new_values.reshape(shaped), prompt_keys.reshape(prompted), prompt_values.reshape(prompted), cache_keys.reshape(cached), cache_values.reshape(cached), cache_lengths.reshape(GROUPS, REQ_DEV), parents.reshape(GROUPS, REQ_DEV, NODES)))
    flattened = attended.reshape(TOKENS, HEADS * HEAD)
    return jnp.dot(flattened, out_weight, preferred_element_type=jnp.float32).astype(jnp.bfloat16)
```

```python
import math

import jax
import jax.numpy as jnp
import numpy as np
from jax import lax
from jax.sharding import Mesh
from jax.sharding import PartitionSpec as P

HEAD = 224
GY = ("gyx", "gyz")


def contract_rows(left, right):
    return lax.dot_general(
        left, right, (((1,), (1,)), ((), ())), preferred_element_type=jnp.float32
    )


def ancestors(parents):
    node_count = parents.shape[1]
    columns = jnp.arange(node_count, dtype=jnp.int32)
    parent_hot = (parents[:, :, None] == columns[None, None, :]).astype(jnp.float32)
    reached = jnp.minimum(jnp.eye(node_count, dtype=jnp.float32)[None] + parent_hot, 1.0)
    rounds = max(1, math.ceil(math.log2(node_count)))
    for sweep in range(rounds):
        reached = jnp.minimum(
            reached + jnp.einsum("rnm,rmk->rnk", reached, reached, precision=lax.Precision.HIGHEST),
            1.0,
        )
    return reached


def attend(queries, new_keys, new_values, prompt_k, prompt_v, cache_k, cache_v, lengths, parents):
    factor = 1.0 / math.sqrt(queries.shape[-1])
    s_prompt = (
        jnp.einsum("rnhe,hep->rnhp", queries, prompt_k, preferred_element_type=jnp.float32) * factor
    )
    s_cache = (
        jnp.einsum("rnhe,rhec->rnhc", queries, cache_k, preferred_element_type=jnp.float32) * factor
    )
    s_tree = (
        jnp.einsum("rnhe,rmhe->rnhm", queries, new_keys, preferred_element_type=jnp.float32)
        * factor
    )
    usable = jnp.arange(cache_k.shape[-1], dtype=jnp.int32)[None, :] < lengths[:, None]
    s_cache = jnp.where(usable[:, None, None, :], s_cache, -jnp.inf)
    reached = ancestors(parents)
    s_tree = jnp.where(reached[:, :, None, :] > 0.5, s_tree, -jnp.inf)
    largest = jnp.maximum(
        jnp.maximum(
            jnp.max(s_prompt, axis=-1, keepdims=True), jnp.max(s_cache, axis=-1, keepdims=True)
        ),
        jnp.max(s_tree, axis=-1, keepdims=True),
    )
    e_prompt = jnp.exp(s_prompt - largest)
    e_cache = jnp.exp(s_cache - largest)
    e_tree = jnp.exp(s_tree - largest)
    totals = (
        jnp.sum(e_prompt, axis=-1, keepdims=True)
        + jnp.sum(e_cache, axis=-1, keepdims=True)
        + jnp.sum(e_tree, axis=-1, keepdims=True)
    )
    w_prompt = (e_prompt / totals).astype(jnp.bfloat16)
    w_cache = (e_cache / totals).astype(jnp.bfloat16)
    w_tree = (e_tree / totals).astype(jnp.bfloat16)
    result = jnp.einsum("rnhp,hep->rnhe", w_prompt, prompt_v, preferred_element_type=jnp.float32)
    result = result + jnp.einsum(
        "rnhc,rhec->rnhe", w_cache, cache_v, preferred_element_type=jnp.float32
    )
    result = result + jnp.einsum(
        "rnhm,rmhe->rnhe", w_tree, new_values, preferred_element_type=jnp.float32
    )
    return result.astype(jnp.bfloat16)


def per_device(
    inputs,
    query_weight,
    key_weight,
    value_weight,
    adapter_down,
    adapter_up,
    prompt_keys,
    prompt_values,
    cache_keys,
    cache_values,
    cache_lengths,
    parents,
    out_weight,
):
    requests = cache_keys.shape[0]
    node_count = parents.shape[1]
    local_rows = requests * node_count
    head_width = query_weight.shape[0]
    full_columns = lax.all_gather(out_weight, "gx", axis=1, tiled=True)
    own_block = lax.all_to_all(full_columns, "gyx", 1, 0, tiled=True)
    all_rows = lax.all_gather(inputs, GY, axis=0, tiled=True)
    mixture = lax.psum_scatter(
        jnp.concatenate(
            [
                contract_rows(all_rows, matrix)
                for matrix in (query_weight, key_weight, value_weight, adapter_down)
            ],
            axis=1,
        ),
        "gx",
        scatter_dimension=0,
        tiled=True,
    )
    head_count = head_width // HEAD
    query_base = mixture[:, :head_width]
    new_keys = mixture[:, head_width : 2 * head_width].astype(jnp.bfloat16)
    new_values = mixture[:, 2 * head_width : 3 * head_width].astype(jnp.bfloat16)
    adapter_mid = mixture[:, 3 * head_width :].astype(jnp.bfloat16)
    queries = (query_base + contract_rows(adapter_mid, adapter_up)).astype(jnp.bfloat16)
    shaped = (requests, node_count, head_count, HEAD)
    cached = (requests, head_count, HEAD, cache_keys.shape[2])
    attended = attend(
        queries.reshape(shaped),
        new_keys.reshape(shaped),
        new_values.reshape(shaped),
        prompt_keys,
        prompt_values,
        cache_keys.reshape(cached),
        cache_values.reshape(cached),
        cache_lengths,
        parents,
    )
    flattened = attended.reshape(local_rows, head_width)
    heads_along_x = lax.all_gather(flattened, "gyx", axis=1, tiled=True)
    partial_sums = jnp.dot(heads_along_x, own_block, preferred_element_type=jnp.float32)
    parts = lax.psum(1, "gyz")
    pieces = partial_sums.astype(jnp.bfloat16).reshape(local_rows, parts, -1)
    arrived = lax.all_to_all(pieces, "gyz", 1, 1, tiled=True)
    return jnp.sum(arrived.astype(jnp.float32), axis=1).astype(jnp.bfloat16)


def split_mesh(mesh):
    devices = mesh.devices
    along_x = len({d.coords[0] for d in devices[0]})
    shape = (devices.shape[0], along_x, devices.shape[1] // along_x)
    return Mesh(devices.reshape(shape), ("gx",) + GY)


def solution(mesh):
    placed = (
        P(GY, "gx"),
        P(GY, "gx"),
        P(GY, "gx"),
        P(GY, "gx"),
        P(None, "gx"),
        P(GY, None),
        P("gx", GY, None),
        P("gx", GY, None),
        P("gx", GY, None),
        P("gx", GY, None),
        P("gx"),
        P("gx", None),
        P(GY, "gx"),
    )
    return jax.shard_map(
        per_device, mesh=split_mesh(mesh), in_specs=placed, out_specs=P("gx", GY), check_vma=False
    )
```

```python
import math

import jax
import jax.numpy as jnp
import numpy as np
from jax import lax
from jax.sharding import Mesh
from jax.sharding import PartitionSpec as P

HEAD = 224
GY = ("gyx", "gyz")


def contract_rows(left, right):
    return lax.dot_general(
        left, right, (((1,), (1,)), ((), ())), preferred_element_type=jnp.float32
    )


def ancestors(parents):
    node_count = parents.shape[1]
    columns = jnp.arange(node_count, dtype=jnp.int32)
    parent_hot = (parents[:, :, None] == columns[None, None, :]).astype(jnp.float32)
    reached = jnp.minimum(jnp.eye(node_count, dtype=jnp.float32)[None] + parent_hot, 1.0)
    rounds = max(1, math.ceil(math.log2(node_count)))
    for sweep in range(rounds):
        reached = jnp.minimum(
            reached + jnp.einsum("rnm,rmk->rnk", reached, reached, precision=lax.Precision.HIGHEST),
            1.0,
        )
    return reached


def attend(queries, new_keys, new_values, prompt_k, prompt_v, cache_k, cache_v, lengths, parents):
    factor = 1.0 / math.sqrt(queries.shape[-1])
    s_prompt = (
        jnp.einsum("rnhe,hep->rnhp", queries, prompt_k, preferred_element_type=jnp.float32) * factor
    )
    s_cache = (
        jnp.einsum("rnhe,rhec->rnhc", queries, cache_k, preferred_element_type=jnp.float32) * factor
    )
    s_tree = (
        jnp.einsum("rnhe,rmhe->rnhm", queries, new_keys, preferred_element_type=jnp.float32)
        * factor
    )
    usable = jnp.arange(cache_k.shape[-1], dtype=jnp.int32)[None, :] < lengths[:, None]
    s_cache = jnp.where(usable[:, None, None, :], s_cache, -jnp.inf)
    reached = ancestors(parents)
    s_tree = jnp.where(reached[:, :, None, :] > 0.5, s_tree, -jnp.inf)
    largest = jnp.maximum(
        jnp.maximum(
            jnp.max(s_prompt, axis=-1, keepdims=True), jnp.max(s_cache, axis=-1, keepdims=True)
        ),
        jnp.max(s_tree, axis=-1, keepdims=True),
    )
    e_prompt = jnp.exp(s_prompt - largest)
    e_cache = jnp.exp(s_cache - largest)
    e_tree = jnp.exp(s_tree - largest)
    totals = (
        jnp.sum(e_prompt, axis=-1, keepdims=True)
        + jnp.sum(e_cache, axis=-1, keepdims=True)
        + jnp.sum(e_tree, axis=-1, keepdims=True)
    )
    w_prompt = (e_prompt / totals).astype(jnp.bfloat16)
    w_cache = (e_cache / totals).astype(jnp.bfloat16)
    w_tree = (e_tree / totals).astype(jnp.bfloat16)
    result = jnp.einsum("rnhp,hep->rnhe", w_prompt, prompt_v, preferred_element_type=jnp.float32)
    result = result + jnp.einsum(
        "rnhc,rhec->rnhe", w_cache, cache_v, preferred_element_type=jnp.float32
    )
    result = result + jnp.einsum(
        "rnhm,rmhe->rnhe", w_tree, new_values, preferred_element_type=jnp.float32
    )
    return result.astype(jnp.bfloat16)


CHUNKS = 1


def gather_like_all_to_all(block, axis_name):
    count = lax.psum(1, axis_name)
    copies = jnp.broadcast_to(block[None], (count,) + block.shape)
    return lax.all_to_all(copies, axis_name, 0, 0, tiled=True)


def per_device(
    inputs,
    query_weight,
    key_weight,
    value_weight,
    adapter_down,
    adapter_up,
    prompt_keys,
    prompt_values,
    cache_keys,
    cache_values,
    cache_lengths,
    parents,
    out_weight,
):
    along_x = lax.psum(1, "gyx")
    along_z = lax.psum(1, "gyz")
    groups = lax.psum(1, "gx")
    node_count = parents.shape[1]
    head_width = query_weight.shape[0]
    head_count = head_width // HEAD
    per_x = groups // along_x
    columns = out_weight.shape[1]
    every_block = gather_like_all_to_all(out_weight, "gx")
    every_block = every_block.reshape(along_x, per_x, head_width, columns)
    own_block = lax.all_to_all(every_block, "gyx", 0, 0, tiled=True)
    own_block = own_block.transpose(0, 2, 1, 3).reshape(along_x * head_width, per_x * columns)
    weights = jnp.concatenate([query_weight, key_weight, value_weight, adapter_down], axis=0)
    local = inputs.shape[0]
    rows = local // CHUNKS
    results = []
    for chunk in range(CHUNKS):
        piece = inputs[chunk * rows : (chunk + 1) * rows]
        gathered = lax.all_gather(lax.all_gather(piece, "gyx", axis=0, tiled=True), "gyz", axis=0, tiled=True)
        partial = contract_rows(gathered, weights).astype(jnp.bfloat16)
        per_group_z = along_z * along_x // groups
        partial = partial.reshape(groups // along_x, per_group_z, along_x, rows, -1)
        partial = partial.transpose(2, 0, 1, 3, 4).reshape(groups, per_group_z * rows, -1)
        arrived = lax.all_to_all(partial, "gx", 0, 0, tiled=True)
        mixture = jnp.sum(arrived.astype(jnp.float32), axis=0)
        query_base = mixture[:, :head_width]
        new_keys = mixture[:, head_width : 2 * head_width].astype(jnp.bfloat16)
        new_values = mixture[:, 2 * head_width : 3 * head_width].astype(jnp.bfloat16)
        adapter_mid = mixture[:, 3 * head_width :].astype(jnp.bfloat16)
        queries = (query_base + contract_rows(adapter_mid, adapter_up)).astype(jnp.bfloat16)
        requests = mixture.shape[0] // node_count
        shaped = (requests, node_count, head_count, HEAD)
        cached = (requests, head_count, HEAD, cache_keys.shape[2])
        attended = attend(
            queries.reshape(shaped),
            new_keys.reshape(shaped),
            new_values.reshape(shaped),
            prompt_keys,
            prompt_values,
            cache_keys[chunk::CHUNKS].reshape(cached),
            cache_values[chunk::CHUNKS].reshape(cached),
            cache_lengths[chunk::CHUNKS],
            parents[chunk::CHUNKS],
        )
        flattened = attended.reshape(requests * node_count, head_width)
        heads_along_x = lax.all_gather(flattened, "gyx", axis=1, tiled=True)
        partial_sums = jnp.dot(heads_along_x, own_block, preferred_element_type=jnp.float32)
        pieces = partial_sums.astype(jnp.bfloat16).reshape(requests * node_count, along_z, -1)
        landed = lax.all_to_all(pieces, "gyz", 1, 1, tiled=True)
        out = jnp.sum(landed.astype(jnp.float32), axis=1).astype(jnp.bfloat16)
        results.append(out.reshape(requests, node_count, -1))
    stacked = jnp.stack(results, axis=1)
    return stacked.reshape(-1, stacked.shape[-1])


def split_mesh(mesh):
    devices = mesh.devices
    along_x = len({d.coords[0] for d in devices[0]})
    shape = (devices.shape[0], along_x, devices.shape[1] // along_x)
    return Mesh(devices.reshape(shape), ("gx",) + GY)


def solution(mesh):
    placed = (
        P(GY, "gx"),
        P(GY, "gx"),
        P(GY, "gx"),
        P(GY, "gx"),
        P(None, "gx"),
        P(GY, None),
        P("gx", GY, None),
        P("gx", GY, None),
        P("gx", GY, None),
        P("gx", GY, None),
        P("gx"),
        P("gx", None),
        P(GY, "gx"),
    )
    return jax.shard_map(
        per_device, mesh=split_mesh(mesh), in_specs=placed, out_specs=P("gx", GY), check_vma=False
    )
```

```python
import math

import jax
import jax.numpy as jnp
import numpy as np
from jax import lax
from jax.sharding import Mesh
from jax.sharding import PartitionSpec as P

HEAD = 224
GY = ("gyx", "gyz")


def contract_rows(left, right):
    return lax.dot_general(
        left, right, (((1,), (1,)), ((), ())), preferred_element_type=jnp.float32
    )


def ancestors(parents):
    node_count = parents.shape[1]
    columns = jnp.arange(node_count, dtype=jnp.int32)
    parent_hot = (parents[:, :, None] == columns[None, None, :]).astype(jnp.float32)
    reached = jnp.minimum(jnp.eye(node_count, dtype=jnp.float32)[None] + parent_hot, 1.0)
    rounds = max(1, math.ceil(math.log2(node_count)))
    for sweep in range(rounds):
        reached = jnp.minimum(
            reached + jnp.einsum("rnm,rmk->rnk", reached, reached, precision=lax.Precision.HIGHEST),
            1.0,
        )
    return reached


def attend(queries, new_keys, new_values, prompt_k, prompt_v, cache_k, cache_v, lengths, parents):
    factor = 1.0 / math.sqrt(queries.shape[-1])
    s_prompt = (
        jnp.einsum("rnhe,hep->rnhp", queries, prompt_k, preferred_element_type=jnp.float32) * factor
    )
    s_cache = (
        jnp.einsum("rnhe,rhec->rnhc", queries, cache_k, preferred_element_type=jnp.float32) * factor
    )
    s_tree = (
        jnp.einsum("rnhe,rmhe->rnhm", queries, new_keys, preferred_element_type=jnp.float32)
        * factor
    )
    usable = jnp.arange(cache_k.shape[-1], dtype=jnp.int32)[None, :] < lengths[:, None]
    s_cache = jnp.where(usable[:, None, None, :], s_cache, -jnp.inf)
    reached = ancestors(parents)
    s_tree = jnp.where(reached[:, :, None, :] > 0.5, s_tree, -jnp.inf)
    largest = jnp.maximum(
        jnp.maximum(
            jnp.max(s_prompt, axis=-1, keepdims=True), jnp.max(s_cache, axis=-1, keepdims=True)
        ),
        jnp.max(s_tree, axis=-1, keepdims=True),
    )
    e_prompt = jnp.exp(s_prompt - largest)
    e_cache = jnp.exp(s_cache - largest)
    e_tree = jnp.exp(s_tree - largest)
    totals = (
        jnp.sum(e_prompt, axis=-1, keepdims=True)
        + jnp.sum(e_cache, axis=-1, keepdims=True)
        + jnp.sum(e_tree, axis=-1, keepdims=True)
    )
    w_prompt = (e_prompt / totals).astype(jnp.bfloat16)
    w_cache = (e_cache / totals).astype(jnp.bfloat16)
    w_tree = (e_tree / totals).astype(jnp.bfloat16)
    result = jnp.einsum("rnhp,hep->rnhe", w_prompt, prompt_v, preferred_element_type=jnp.float32)
    result = result + jnp.einsum(
        "rnhc,rhec->rnhe", w_cache, cache_v, preferred_element_type=jnp.float32
    )
    result = result + jnp.einsum(
        "rnhm,rmhe->rnhe", w_tree, new_values, preferred_element_type=jnp.float32
    )
    return result.astype(jnp.bfloat16)


CHUNKS = 1


def gather_like_all_to_all(block, axis_name):
    count = lax.psum(1, axis_name)
    copies = jnp.broadcast_to(block[None], (count,) + block.shape)
    return lax.all_to_all(copies, axis_name, 0, 0, tiled=True)


def per_device(
    inputs,
    query_weight,
    key_weight,
    value_weight,
    adapter_down,
    adapter_up,
    prompt_keys,
    prompt_values,
    cache_keys,
    cache_values,
    cache_lengths,
    parents,
    out_weight,
):
    along_x = lax.psum(1, "gyx")
    along_z = lax.psum(1, "gyz")
    groups = lax.psum(1, "gx")
    node_count = parents.shape[1]
    head_width = query_weight.shape[0]
    head_count = head_width // HEAD
    per_x = groups // along_x
    columns = out_weight.shape[1]
    every_block = gather_like_all_to_all(out_weight, "gx")
    every_block = every_block.reshape(along_x, per_x, head_width, columns)
    own_block = lax.all_to_all(every_block, "gyx", 0, 0, tiled=True)
    own_block = own_block.transpose(0, 2, 1, 3).reshape(along_x * head_width, per_x * columns)
    weights = jnp.concatenate([query_weight, key_weight, value_weight, adapter_down], axis=0)
    local = inputs.shape[0]
    rows = local // CHUNKS
    results = []
    for chunk in range(CHUNKS):
        piece = inputs[chunk * rows : (chunk + 1) * rows]
        gathered = lax.all_gather(piece, GY, axis=0, tiled=True)
        partial = contract_rows(gathered, weights).astype(jnp.bfloat16)
        mixture = lax.psum_scatter(partial, "gx", scatter_dimension=0, tiled=True).astype(jnp.float32)
        query_base = mixture[:, :head_width]
        new_keys = mixture[:, head_width : 2 * head_width].astype(jnp.bfloat16)
        new_values = mixture[:, 2 * head_width : 3 * head_width].astype(jnp.bfloat16)
        adapter_mid = mixture[:, 3 * head_width :].astype(jnp.bfloat16)
        queries = (query_base + contract_rows(adapter_mid, adapter_up)).astype(jnp.bfloat16)
        requests = mixture.shape[0] // node_count
        shaped = (requests, node_count, head_count, HEAD)
        cached = (requests, head_count, HEAD, cache_keys.shape[2])
        attended = attend(
            queries.reshape(shaped),
            new_keys.reshape(shaped),
            new_values.reshape(shaped),
            prompt_keys,
            prompt_values,
            cache_keys[chunk::CHUNKS].reshape(cached),
            cache_values[chunk::CHUNKS].reshape(cached),
            cache_lengths[chunk::CHUNKS],
            parents[chunk::CHUNKS],
        )
        flattened = attended.reshape(requests * node_count, head_width)
        heads_along_x = lax.all_gather(flattened, "gyx", axis=1, tiled=True)
        partial_sums = jnp.dot(heads_along_x, own_block, preferred_element_type=jnp.float32)
        pieces = partial_sums.astype(jnp.bfloat16).reshape(requests * node_count, along_z, -1)
        landed = lax.all_to_all(pieces, "gyz", 1, 1, tiled=True)
        out = jnp.sum(landed.astype(jnp.float32), axis=1).astype(jnp.bfloat16)
        results.append(out.reshape(requests, node_count, -1))
    stacked = jnp.stack(results, axis=1)
    return stacked.reshape(-1, stacked.shape[-1])


def split_mesh(mesh):
    devices = mesh.devices
    along_x = len({d.coords[0] for d in devices[0]})
    shape = (devices.shape[0], along_x, devices.shape[1] // along_x)
    return Mesh(devices.reshape(shape), ("gx",) + GY)


def solution(mesh):
    placed = (
        P(GY, "gx"),
        P(GY, "gx"),
        P(GY, "gx"),
        P(GY, "gx"),
        P(None, "gx"),
        P(GY, None),
        P("gx", GY, None),
        P("gx", GY, None),
        P("gx", GY, None),
        P("gx", GY, None),
        P("gx"),
        P("gx", None),
        P(GY, "gx"),
    )
    return jax.shard_map(
        per_device, mesh=split_mesh(mesh), in_specs=placed, out_specs=P("gx", GY), check_vma=False
    )
```

```python
import math

import jax
import jax.numpy as jnp
import numpy as np
from jax import lax
from jax.sharding import Mesh
from jax.sharding import PartitionSpec as P

HEAD = 224
GY = ("gyx", "gyz")


def contract_rows(left, right):
    return lax.dot_general(
        left, right, (((1,), (1,)), ((), ())), preferred_element_type=jnp.float32
    )


def ancestors(parents):
    node_count = parents.shape[1]
    columns = jnp.arange(node_count, dtype=jnp.int32)
    parent_hot = (parents[:, :, None] == columns[None, None, :]).astype(jnp.float32)
    reached = jnp.minimum(jnp.eye(node_count, dtype=jnp.float32)[None] + parent_hot, 1.0)
    rounds = max(1, math.ceil(math.log2(node_count)))
    for sweep in range(rounds):
        reached = jnp.minimum(
            reached + jnp.einsum("rnm,rmk->rnk", reached, reached, precision=lax.Precision.HIGHEST),
            1.0,
        )
    return reached


def attend(queries, new_keys, new_values, prompt_k, prompt_v, cache_k, cache_v, lengths, parents):
    factor = 1.0 / math.sqrt(queries.shape[-1])
    s_prompt = (
        jnp.einsum("rnhe,hep->rnhp", queries, prompt_k, preferred_element_type=jnp.float32) * factor
    )
    s_cache = (
        jnp.einsum("rnhe,rhec->rnhc", queries, cache_k, preferred_element_type=jnp.float32) * factor
    )
    s_tree = (
        jnp.einsum("rnhe,rmhe->rnhm", queries, new_keys, preferred_element_type=jnp.float32)
        * factor
    )
    usable = jnp.arange(cache_k.shape[-1], dtype=jnp.int32)[None, :] < lengths[:, None]
    s_cache = jnp.where(usable[:, None, None, :], s_cache, -jnp.inf)
    reached = ancestors(parents)
    s_tree = jnp.where(reached[:, :, None, :] > 0.5, s_tree, -jnp.inf)
    largest = jnp.maximum(
        jnp.maximum(
            jnp.max(s_prompt, axis=-1, keepdims=True), jnp.max(s_cache, axis=-1, keepdims=True)
        ),
        jnp.max(s_tree, axis=-1, keepdims=True),
    )
    e_prompt = jnp.exp(s_prompt - largest)
    e_cache = jnp.exp(s_cache - largest)
    e_tree = jnp.exp(s_tree - largest)
    totals = (
        jnp.sum(e_prompt, axis=-1, keepdims=True)
        + jnp.sum(e_cache, axis=-1, keepdims=True)
        + jnp.sum(e_tree, axis=-1, keepdims=True)
    )
    w_prompt = (e_prompt / totals).astype(jnp.bfloat16)
    w_cache = (e_cache / totals).astype(jnp.bfloat16)
    w_tree = (e_tree / totals).astype(jnp.bfloat16)
    result = jnp.einsum("rnhp,hep->rnhe", w_prompt, prompt_v, preferred_element_type=jnp.float32)
    result = result + jnp.einsum(
        "rnhc,rhec->rnhe", w_cache, cache_v, preferred_element_type=jnp.float32
    )
    result = result + jnp.einsum(
        "rnhm,rmhe->rnhe", w_tree, new_values, preferred_element_type=jnp.float32
    )
    return result.astype(jnp.bfloat16)


CHUNKS = 1


def gather_like_all_to_all(block, axis_name):
    count = lax.psum(1, axis_name)
    copies = jnp.broadcast_to(block[None], (count,) + block.shape)
    return lax.all_to_all(copies, axis_name, 0, 0, tiled=True)


def per_device(
    inputs,
    query_weight,
    key_weight,
    value_weight,
    adapter_down,
    adapter_up,
    prompt_keys,
    prompt_values,
    cache_keys,
    cache_values,
    cache_lengths,
    parents,
    out_weight,
):
    along_x = lax.psum(1, "gyx")
    along_z = lax.psum(1, "gyz")
    groups = lax.psum(1, "gx")
    node_count = parents.shape[1]
    head_width = query_weight.shape[0]
    head_count = head_width // HEAD
    per_x = groups // along_x
    columns = out_weight.shape[1]
    every_block = gather_like_all_to_all(out_weight, "gx")
    every_block = every_block.reshape(along_x, per_x, head_width, columns)
    own_block = lax.all_to_all(every_block, "gyx", 0, 0, tiled=True)
    weights = (query_weight, key_weight, value_weight, adapter_down)
    local = inputs.shape[0]
    rows = local // CHUNKS
    results = []
    for chunk in range(CHUNKS):
        piece = inputs[chunk * rows : (chunk + 1) * rows]
        gathered = lax.all_gather(piece, GY, axis=0, tiled=True)
        if chunk == 0:
            gathered, own_block = lax.optimization_barrier((gathered, own_block))
        mixture = lax.psum_scatter(
            jnp.concatenate([contract_rows(gathered, matrix) for matrix in weights], axis=1),
            "gx",
            scatter_dimension=0,
            tiled=True,
        )
        query_base = mixture[:, :head_width]
        new_keys = mixture[:, head_width : 2 * head_width].astype(jnp.bfloat16)
        new_values = mixture[:, 2 * head_width : 3 * head_width].astype(jnp.bfloat16)
        adapter_mid = mixture[:, 3 * head_width :].astype(jnp.bfloat16)
        queries = (query_base + contract_rows(adapter_mid, adapter_up)).astype(jnp.bfloat16)
        requests = mixture.shape[0] // node_count
        shaped = (requests, node_count, head_count, HEAD)
        cached = (requests, head_count, HEAD, cache_keys.shape[2])
        attended = attend(
            queries.reshape(shaped),
            new_keys.reshape(shaped),
            new_values.reshape(shaped),
            prompt_keys,
            prompt_values,
            cache_keys[chunk::CHUNKS].reshape(cached),
            cache_values[chunk::CHUNKS].reshape(cached),
            cache_lengths[chunk::CHUNKS],
            parents[chunk::CHUNKS],
        )
        flattened = attended.reshape(requests * node_count, head_width)
        heads_along_x = lax.all_gather(flattened, "gyx", axis=1, tiled=True)
        heads_along_x = heads_along_x.reshape(requests * node_count, along_x, head_width)
        partial_sums = jnp.einsum(
            "txe,xkec->tkc", heads_along_x, own_block, preferred_element_type=jnp.float32
        )
        pieces = partial_sums.astype(jnp.bfloat16).reshape(requests * node_count, along_z, -1)
        landed = lax.all_to_all(pieces, "gyz", 1, 1, tiled=True)
        out = jnp.sum(landed.astype(jnp.float32), axis=1).astype(jnp.bfloat16)
        results.append(out.reshape(requests, node_count, -1))
    stacked = jnp.stack(results, axis=1)
    return stacked.reshape(-1, stacked.shape[-1])


def split_mesh(mesh):
    devices = mesh.devices
    along_x = len({d.coords[0] for d in devices[0]})
    shape = (devices.shape[0], along_x, devices.shape[1] // along_x)
    return Mesh(devices.reshape(shape), ("gx",) + GY)


def solution(mesh):
    placed = (
        P(GY, "gx"),
        P(GY, "gx"),
        P(GY, "gx"),
        P(GY, "gx"),
        P(None, "gx"),
        P(GY, None),
        P("gx", GY, None),
        P("gx", GY, None),
        P("gx", GY, None),
        P("gx", GY, None),
        P("gx"),
        P("gx", None),
        P(GY, "gx"),
    )
    return jax.shard_map(
        per_device, mesh=split_mesh(mesh), in_specs=placed, out_specs=P("gx", GY), check_vma=False
    )
```

```python
import math

import jax
import jax.numpy as jnp
import numpy as np
from jax import lax
from jax.sharding import Mesh
from jax.sharding import PartitionSpec as P

HEAD = 224
GY = ("gyx", "gyz")


def contract_rows(left, right):
    return lax.dot_general(
        left, right, (((1,), (1,)), ((), ())), preferred_element_type=jnp.float32
    )


def ancestors(parents):
    node_count = parents.shape[1]
    columns = jnp.arange(node_count, dtype=jnp.int32)
    parent_hot = (parents[:, :, None] == columns[None, None, :]).astype(jnp.float32)
    reached = jnp.minimum(jnp.eye(node_count, dtype=jnp.float32)[None] + parent_hot, 1.0)
    rounds = max(1, math.ceil(math.log2(node_count)))
    for sweep in range(rounds):
        reached = jnp.minimum(
            reached + jnp.einsum("rnm,rmk->rnk", reached, reached, precision=lax.Precision.HIGHEST),
            1.0,
        )
    return reached


def attend(queries, new_keys, new_values, prompt_k, prompt_v, cache_k, cache_v, lengths, parents):
    factor = 1.0 / math.sqrt(queries.shape[-1])
    s_prompt = (
        jnp.einsum("rnhe,hep->rnhp", queries, prompt_k, preferred_element_type=jnp.float32) * factor
    )
    s_cache = (
        jnp.einsum("rnhe,rhec->rnhc", queries, cache_k, preferred_element_type=jnp.float32) * factor
    )
    s_tree = (
        jnp.einsum("rnhe,rmhe->rnhm", queries, new_keys, preferred_element_type=jnp.float32)
        * factor
    )
    usable = jnp.arange(cache_k.shape[-1], dtype=jnp.int32)[None, :] < lengths[:, None]
    s_cache = jnp.where(usable[:, None, None, :], s_cache, -jnp.inf)
    reached = ancestors(parents)
    s_tree = jnp.where(reached[:, :, None, :] > 0.5, s_tree, -jnp.inf)
    largest = jnp.maximum(
        jnp.maximum(
            jnp.max(s_prompt, axis=-1, keepdims=True), jnp.max(s_cache, axis=-1, keepdims=True)
        ),
        jnp.max(s_tree, axis=-1, keepdims=True),
    )
    e_prompt = jnp.exp(s_prompt - largest)
    e_cache = jnp.exp(s_cache - largest)
    e_tree = jnp.exp(s_tree - largest)
    totals = (
        jnp.sum(e_prompt, axis=-1, keepdims=True)
        + jnp.sum(e_cache, axis=-1, keepdims=True)
        + jnp.sum(e_tree, axis=-1, keepdims=True)
    )
    w_prompt = (e_prompt / totals).astype(jnp.bfloat16)
    w_cache = (e_cache / totals).astype(jnp.bfloat16)
    w_tree = (e_tree / totals).astype(jnp.bfloat16)
    result = jnp.einsum("rnhp,hep->rnhe", w_prompt, prompt_v, preferred_element_type=jnp.float32)
    result = result + jnp.einsum(
        "rnhc,rhec->rnhe", w_cache, cache_v, preferred_element_type=jnp.float32
    )
    result = result + jnp.einsum(
        "rnhm,rmhe->rnhe", w_tree, new_values, preferred_element_type=jnp.float32
    )
    return result.astype(jnp.bfloat16)


CHUNKS = 2


def gather_like_all_to_all(block, axis_name):
    count = lax.psum(1, axis_name)
    copies = jnp.broadcast_to(block[None], (count,) + block.shape)
    return lax.all_to_all(copies, axis_name, 0, 0, tiled=True)


def per_device(
    inputs,
    query_weight,
    key_weight,
    value_weight,
    adapter_down,
    adapter_up,
    prompt_keys,
    prompt_values,
    cache_keys,
    cache_values,
    cache_lengths,
    parents,
    out_weight,
):
    along_x = lax.psum(1, "gyx")
    along_z = lax.psum(1, "gyz")
    groups = lax.psum(1, "gx")
    node_count = parents.shape[1]
    head_width = query_weight.shape[0]
    head_count = head_width // HEAD
    per_x = groups // along_x
    columns = out_weight.shape[1]
    every_block = gather_like_all_to_all(out_weight, "gx")
    every_block = every_block.reshape(along_x, per_x, head_width, columns)
    own_block = lax.all_to_all(every_block, "gyx", 0, 0, tiled=True)
    weights = (query_weight, key_weight, value_weight, adapter_down)
    local = inputs.shape[0]
    rows = local // CHUNKS
    results = []
    for chunk in range(CHUNKS):
        piece = inputs[chunk * rows : (chunk + 1) * rows]
        gathered = lax.all_gather(piece, GY, axis=0, tiled=True)
        if chunk == CHUNKS - 1:
            gathered, own_block = lax.optimization_barrier((gathered, own_block))
        mixture = lax.psum_scatter(
            jnp.concatenate([contract_rows(gathered, matrix) for matrix in weights], axis=1),
            "gx",
            scatter_dimension=0,
            tiled=True,
        )
        query_base = mixture[:, :head_width]
        new_keys = mixture[:, head_width : 2 * head_width].astype(jnp.bfloat16)
        new_values = mixture[:, 2 * head_width : 3 * head_width].astype(jnp.bfloat16)
        adapter_mid = mixture[:, 3 * head_width :].astype(jnp.bfloat16)
        queries = (query_base + contract_rows(adapter_mid, adapter_up)).astype(jnp.bfloat16)
        requests = mixture.shape[0] // node_count
        shaped = (requests, node_count, head_count, HEAD)
        cached = (requests, head_count, HEAD, cache_keys.shape[2])
        attended = attend(
            queries.reshape(shaped),
            new_keys.reshape(shaped),
            new_values.reshape(shaped),
            prompt_keys,
            prompt_values,
            cache_keys[chunk::CHUNKS].reshape(cached),
            cache_values[chunk::CHUNKS].reshape(cached),
            cache_lengths[chunk::CHUNKS],
            parents[chunk::CHUNKS],
        )
        flattened = attended.reshape(requests * node_count, head_width)
        heads_along_x = lax.all_gather(flattened, "gyx", axis=1, tiled=True)
        heads_along_x = heads_along_x.reshape(requests * node_count, along_x, head_width)
        partial_sums = jnp.einsum(
            "txe,xkec->tkc", heads_along_x, own_block, preferred_element_type=jnp.float32
        )
        pieces = partial_sums.astype(jnp.bfloat16).reshape(requests * node_count, along_z, -1)
        landed = lax.all_to_all(pieces, "gyz", 1, 1, tiled=True)
        out = jnp.sum(landed.astype(jnp.float32), axis=1).astype(jnp.bfloat16)
        results.append(out.reshape(requests, node_count, -1))
    stacked = jnp.stack(results, axis=1)
    return stacked.reshape(-1, stacked.shape[-1])


def split_mesh(mesh):
    devices = mesh.devices
    along_x = len({d.coords[0] for d in devices[0]})
    shape = (devices.shape[0], along_x, devices.shape[1] // along_x)
    return Mesh(devices.reshape(shape), ("gx",) + GY)


def solution(mesh):
    placed = (
        P(GY, "gx"),
        P(GY, "gx"),
        P(GY, "gx"),
        P(GY, "gx"),
        P(None, "gx"),
        P(GY, None),
        P("gx", GY, None),
        P("gx", GY, None),
        P("gx", GY, None),
        P("gx", GY, None),
        P("gx"),
        P("gx", None),
        P(GY, "gx"),
    )
    return jax.shard_map(
        per_device, mesh=split_mesh(mesh), in_specs=placed, out_specs=P("gx", GY), check_vma=False
    )
```

```python
import math

import jax
import jax.numpy as jnp
import numpy as np
from jax import lax
from jax.sharding import Mesh
from jax.sharding import PartitionSpec as P

HEAD = 224
GY = ("gyx", "gyz")


def contract_rows(left, right):
    return lax.dot_general(
        left, right, (((1,), (1,)), ((), ())), preferred_element_type=jnp.float32
    )


def ancestors(parents):
    node_count = parents.shape[1]
    columns = jnp.arange(node_count, dtype=jnp.int32)
    parent_hot = (parents[:, :, None] == columns[None, None, :]).astype(jnp.float32)
    reached = jnp.minimum(jnp.eye(node_count, dtype=jnp.float32)[None] + parent_hot, 1.0)
    rounds = max(1, math.ceil(math.log2(node_count)))
    for sweep in range(rounds):
        reached = jnp.minimum(
            reached + jnp.einsum("rnm,rmk->rnk", reached, reached, precision=lax.Precision.HIGHEST),
            1.0,
        )
    return reached


def attend(queries, new_keys, new_values, prompt_k, prompt_v, cache_k, cache_v, lengths, parents):
    factor = 1.0 / math.sqrt(queries.shape[-1])
    s_prompt = (
        jnp.einsum("rnhe,hep->rnhp", queries, prompt_k, preferred_element_type=jnp.float32) * factor
    )
    s_cache = (
        jnp.einsum("rnhe,rhec->rnhc", queries, cache_k, preferred_element_type=jnp.float32) * factor
    )
    s_tree = (
        jnp.einsum("rnhe,rmhe->rnhm", queries, new_keys, preferred_element_type=jnp.float32)
        * factor
    )
    usable = jnp.arange(cache_k.shape[-1], dtype=jnp.int32)[None, :] < lengths[:, None]
    s_cache = jnp.where(usable[:, None, None, :], s_cache, -jnp.inf)
    reached = ancestors(parents)
    s_tree = jnp.where(reached[:, :, None, :] > 0.5, s_tree, -jnp.inf)
    largest = jnp.maximum(
        jnp.maximum(
            jnp.max(s_prompt, axis=-1, keepdims=True), jnp.max(s_cache, axis=-1, keepdims=True)
        ),
        jnp.max(s_tree, axis=-1, keepdims=True),
    )
    e_prompt = jnp.exp(s_prompt - largest)
    e_cache = jnp.exp(s_cache - largest)
    e_tree = jnp.exp(s_tree - largest)
    totals = (
        jnp.sum(e_prompt, axis=-1, keepdims=True)
        + jnp.sum(e_cache, axis=-1, keepdims=True)
        + jnp.sum(e_tree, axis=-1, keepdims=True)
    )
    w_prompt = (e_prompt / totals).astype(jnp.bfloat16)
    w_cache = (e_cache / totals).astype(jnp.bfloat16)
    w_tree = (e_tree / totals).astype(jnp.bfloat16)
    result = jnp.einsum("rnhp,hep->rnhe", w_prompt, prompt_v, preferred_element_type=jnp.float32)
    result = result + jnp.einsum(
        "rnhc,rhec->rnhe", w_cache, cache_v, preferred_element_type=jnp.float32
    )
    result = result + jnp.einsum(
        "rnhm,rmhe->rnhe", w_tree, new_values, preferred_element_type=jnp.float32
    )
    return result.astype(jnp.bfloat16)


CHUNKS = 1


def gather_like_all_to_all(block, axis_name):
    count = lax.psum(1, axis_name)
    copies = jnp.broadcast_to(block[None], (count,) + block.shape)
    return lax.all_to_all(copies, axis_name, 0, 0, tiled=True)


def per_device(
    inputs,
    query_weight,
    key_weight,
    value_weight,
    adapter_down,
    adapter_up,
    prompt_keys,
    prompt_values,
    cache_keys,
    cache_values,
    cache_lengths,
    parents,
    out_weight,
):
    along_x = lax.psum(1, "gyx")
    along_z = lax.psum(1, "gyz")
    groups = lax.psum(1, "gx")
    node_count = parents.shape[1]
    head_width = query_weight.shape[0]
    head_count = head_width // HEAD
    per_x = groups // along_x
    columns = out_weight.shape[1]
    every_block = gather_like_all_to_all(out_weight, "gx")
    every_block = every_block.reshape(along_x, per_x, head_width, columns)
    own_block = lax.all_to_all(every_block, "gyx", 0, 0, tiled=True)
    folded = jnp.dot(adapter_up, adapter_down, preferred_element_type=jnp.float32)
    folded = (query_weight.astype(jnp.float32) + folded).astype(jnp.bfloat16)
    weights = jnp.concatenate([folded, key_weight, value_weight], axis=0)
    local = inputs.shape[0]
    rows = local // CHUNKS
    results = []
    for chunk in range(CHUNKS):
        piece = inputs[chunk * rows : (chunk + 1) * rows]
        gathered = lax.all_gather(piece, GY, axis=0, tiled=True)
        if chunk == CHUNKS - 1:
            gathered, own_block, weights = lax.optimization_barrier((gathered, own_block, weights))
        mixture = lax.psum_scatter(
            contract_rows(gathered, weights),
            "gx",
            scatter_dimension=0,
            tiled=True,
        )
        queries = mixture[:, :head_width].astype(jnp.bfloat16)
        new_keys = mixture[:, head_width : 2 * head_width].astype(jnp.bfloat16)
        new_values = mixture[:, 2 * head_width :].astype(jnp.bfloat16)
        requests = mixture.shape[0] // node_count
        shaped = (requests, node_count, head_count, HEAD)
        cached = (requests, head_count, HEAD, cache_keys.shape[2])
        attended = attend(
            queries.reshape(shaped),
            new_keys.reshape(shaped),
            new_values.reshape(shaped),
            prompt_keys,
            prompt_values,
            cache_keys[chunk::CHUNKS].reshape(cached),
            cache_values[chunk::CHUNKS].reshape(cached),
            cache_lengths[chunk::CHUNKS],
            parents[chunk::CHUNKS],
        )
        flattened = attended.reshape(requests * node_count, head_width)
        heads_along_x = lax.all_gather(flattened, "gyx", axis=1, tiled=True)
        heads_along_x = heads_along_x.reshape(requests * node_count, along_x, head_width)
        partial_sums = jnp.einsum(
            "txe,xkec->tkc", heads_along_x, own_block, preferred_element_type=jnp.float32
        )
        pieces = partial_sums.astype(jnp.bfloat16).reshape(requests * node_count, along_z, -1)
        landed = lax.all_to_all(pieces, "gyz", 1, 1, tiled=True)
        out = jnp.sum(landed.astype(jnp.float32), axis=1).astype(jnp.bfloat16)
        results.append(out.reshape(requests, node_count, -1))
    stacked = jnp.stack(results, axis=1)
    return stacked.reshape(-1, stacked.shape[-1])


def split_mesh(mesh):
    devices = mesh.devices
    along_x = len({d.coords[0] for d in devices[0]})
    shape = (devices.shape[0], along_x, devices.shape[1] // along_x)
    return Mesh(devices.reshape(shape), ("gx",) + GY)


def solution(mesh):
    placed = (
        P(GY, "gx"),
        P(GY, "gx"),
        P(GY, "gx"),
        P(GY, "gx"),
        P(None, "gx"),
        P(GY, None),
        P("gx", GY, None),
        P("gx", GY, None),
        P("gx", GY, None),
        P("gx", GY, None),
        P("gx"),
        P("gx", None),
        P(GY, "gx"),
    )
    return jax.shard_map(
        per_device, mesh=split_mesh(mesh), in_specs=placed, out_specs=P("gx", GY), check_vma=False
    )
```

```python
import math

import jax
import jax.numpy as jnp
import numpy as np
from jax import lax
from jax.sharding import Mesh
from jax.sharding import PartitionSpec as P

HEAD = 224
GY = ("gyx", "gyz")


def contract_rows(left, right):
    return lax.dot_general(
        left, right, (((1,), (1,)), ((), ())), preferred_element_type=jnp.float32
    )


def ancestors(parents):
    node_count = parents.shape[1]
    columns = jnp.arange(node_count, dtype=jnp.int32)
    parent_hot = (parents[:, :, None] == columns[None, None, :]).astype(jnp.float32)
    reached = jnp.minimum(jnp.eye(node_count, dtype=jnp.float32)[None] + parent_hot, 1.0)
    rounds = max(1, math.ceil(math.log2(node_count)))
    for sweep in range(rounds):
        reached = jnp.minimum(
            reached + jnp.einsum("rnm,rmk->rnk", reached, reached, precision=lax.Precision.HIGHEST),
            1.0,
        )
    return reached


def attend(queries, new_keys, new_values, prompt_k, prompt_v, cache_k, cache_v, lengths, parents):
    factor = 1.0 / math.sqrt(queries.shape[-1])
    s_prompt = (
        jnp.einsum("rnhe,hep->rnhp", queries, prompt_k, preferred_element_type=jnp.float32) * factor
    )
    s_cache = (
        jnp.einsum("rnhe,rhec->rnhc", queries, cache_k, preferred_element_type=jnp.float32) * factor
    )
    s_tree = (
        jnp.einsum("rnhe,rmhe->rnhm", queries, new_keys, preferred_element_type=jnp.float32)
        * factor
    )
    usable = jnp.arange(cache_k.shape[-1], dtype=jnp.int32)[None, :] < lengths[:, None]
    s_cache = jnp.where(usable[:, None, None, :], s_cache, -jnp.inf)
    reached = ancestors(parents)
    s_tree = jnp.where(reached[:, :, None, :] > 0.5, s_tree, -jnp.inf)
    largest = jnp.maximum(
        jnp.maximum(
            jnp.max(s_prompt, axis=-1, keepdims=True), jnp.max(s_cache, axis=-1, keepdims=True)
        ),
        jnp.max(s_tree, axis=-1, keepdims=True),
    )
    e_prompt = jnp.exp(s_prompt - largest)
    e_cache = jnp.exp(s_cache - largest)
    e_tree = jnp.exp(s_tree - largest)
    totals = (
        jnp.sum(e_prompt, axis=-1, keepdims=True)
        + jnp.sum(e_cache, axis=-1, keepdims=True)
        + jnp.sum(e_tree, axis=-1, keepdims=True)
    )
    w_prompt = (e_prompt / totals).astype(jnp.bfloat16)
    w_cache = (e_cache / totals).astype(jnp.bfloat16)
    w_tree = (e_tree / totals).astype(jnp.bfloat16)
    result = jnp.einsum("rnhp,hep->rnhe", w_prompt, prompt_v, preferred_element_type=jnp.float32)
    result = result + jnp.einsum(
        "rnhc,rhec->rnhe", w_cache, cache_v, preferred_element_type=jnp.float32
    )
    result = result + jnp.einsum(
        "rnhm,rmhe->rnhe", w_tree, new_values, preferred_element_type=jnp.float32
    )
    return result.astype(jnp.bfloat16)


CHUNKS = 1


def gather_like_all_to_all(block, axis_name):
    count = lax.psum(1, axis_name)
    copies = jnp.broadcast_to(block[None], (count,) + block.shape)
    return lax.all_to_all(copies, axis_name, 0, 0, tiled=True)


def per_device(
    inputs,
    query_weight,
    key_weight,
    value_weight,
    adapter_down,
    adapter_up,
    prompt_keys,
    prompt_values,
    cache_keys,
    cache_values,
    cache_lengths,
    parents,
    out_weight,
):
    along_x = lax.psum(1, "gyx")
    along_z = lax.psum(1, "gyz")
    groups = lax.psum(1, "gx")
    node_count = parents.shape[1]
    head_width = query_weight.shape[0]
    head_count = head_width // HEAD
    per_x = groups // along_x
    columns = out_weight.shape[1]
    every_block = gather_like_all_to_all(out_weight, "gx")
    every_block = every_block.reshape(along_x, per_x, head_width, columns)
    own_block = lax.all_to_all(every_block, "gyx", 0, 0, tiled=True)
    folded = jnp.dot(adapter_up, adapter_down, preferred_element_type=jnp.float32)
    folded = (query_weight.astype(jnp.float32) + folded).astype(jnp.bfloat16)
    weights = jnp.concatenate([folded, key_weight, value_weight], axis=0)
    local = inputs.shape[0]
    rows = local // CHUNKS
    results = []
    for chunk in range(CHUNKS):
        piece = inputs[chunk * rows : (chunk + 1) * rows]
        gathered = lax.all_gather(piece, GY, axis=0, tiled=True)
        if chunk == CHUNKS - 1:
            gathered, own_block, weights = lax.optimization_barrier((gathered, own_block, weights))
        mixture = lax.psum_scatter(
            contract_rows(gathered, weights),
            "gx",
            scatter_dimension=0,
            tiled=True,
        )
        queries = mixture[:, :head_width].astype(jnp.bfloat16)
        new_keys = mixture[:, head_width : 2 * head_width].astype(jnp.bfloat16)
        new_values = mixture[:, 2 * head_width :].astype(jnp.bfloat16)
        requests = mixture.shape[0] // node_count
        shaped = (requests, node_count, head_count, HEAD)
        cached = (requests, head_count, HEAD, cache_keys.shape[2])
        attended = attend(
            queries.reshape(shaped),
            new_keys.reshape(shaped),
            new_values.reshape(shaped),
            prompt_keys,
            prompt_values,
            cache_keys[chunk::CHUNKS].reshape(cached),
            cache_values[chunk::CHUNKS].reshape(cached),
            cache_lengths[chunk::CHUNKS],
            parents[chunk::CHUNKS],
        )
        flattened = attended.reshape(requests * node_count, head_width)
        heads_along_x = gather_like_all_to_all(flattened, "gyx")
        partial_sums = jnp.einsum(
            "xte,xkec->tkc", heads_along_x, own_block, preferred_element_type=jnp.float32
        )
        pieces = partial_sums.astype(jnp.bfloat16).reshape(requests * node_count, along_z, -1)
        landed = lax.all_to_all(pieces, "gyz", 1, 1, tiled=True)
        out = jnp.sum(landed.astype(jnp.float32), axis=1).astype(jnp.bfloat16)
        results.append(out.reshape(requests, node_count, -1))
    stacked = jnp.stack(results, axis=1)
    return stacked.reshape(-1, stacked.shape[-1])


def split_mesh(mesh):
    devices = mesh.devices
    along_x = len({d.coords[0] for d in devices[0]})
    shape = (devices.shape[0], along_x, devices.shape[1] // along_x)
    return Mesh(devices.reshape(shape), ("gx",) + GY)


def solution(mesh):
    placed = (
        P(GY, "gx"),
        P(GY, "gx"),
        P(GY, "gx"),
        P(GY, "gx"),
        P(None, "gx"),
        P(GY, None),
        P("gx", GY, None),
        P("gx", GY, None),
        P("gx", GY, None),
        P("gx", GY, None),
        P("gx"),
        P("gx", None),
        P(GY, "gx"),
    )
    return jax.shard_map(
        per_device, mesh=split_mesh(mesh), in_specs=placed, out_specs=P("gx", GY), check_vma=False
    )
```

```python
import math

import jax
import jax.numpy as jnp
import numpy as np
from jax import lax
from jax.sharding import Mesh
from jax.sharding import PartitionSpec as P

HEAD = 224
GY = ("gyx", "gyz")


def contract_rows(left, right):
    return lax.dot_general(
        left, right, (((1,), (1,)), ((), ())), preferred_element_type=jnp.float32
    )


def ancestors(parents):
    node_count = parents.shape[1]
    columns = jnp.arange(node_count, dtype=jnp.int32)
    parent_hot = (parents[:, :, None] == columns[None, None, :]).astype(jnp.float32)
    reached = jnp.minimum(jnp.eye(node_count, dtype=jnp.float32)[None] + parent_hot, 1.0)
    rounds = max(1, math.ceil(math.log2(node_count)))
    for sweep in range(rounds):
        reached = jnp.minimum(
            reached + jnp.einsum("rnm,rmk->rnk", reached, reached, precision=lax.Precision.HIGHEST),
            1.0,
        )
    return reached


def attend(queries, new_keys, new_values, prompt_k, prompt_v, cache_k, cache_v, lengths, parents):
    factor = 1.0 / math.sqrt(queries.shape[-1])
    s_prompt = (
        jnp.einsum("rnhe,hep->rnhp", queries, prompt_k, preferred_element_type=jnp.float32) * factor
    )
    s_cache = (
        jnp.einsum("rnhe,rhec->rnhc", queries, cache_k, preferred_element_type=jnp.float32) * factor
    )
    s_tree = (
        jnp.einsum("rnhe,rmhe->rnhm", queries, new_keys, preferred_element_type=jnp.float32)
        * factor
    )
    usable = jnp.arange(cache_k.shape[-1], dtype=jnp.int32)[None, :] < lengths[:, None]
    s_cache = jnp.where(usable[:, None, None, :], s_cache, -jnp.inf)
    reached = ancestors(parents)
    s_tree = jnp.where(reached[:, :, None, :] > 0.5, s_tree, -jnp.inf)
    largest = jnp.maximum(
        jnp.maximum(
            jnp.max(s_prompt, axis=-1, keepdims=True), jnp.max(s_cache, axis=-1, keepdims=True)
        ),
        jnp.max(s_tree, axis=-1, keepdims=True),
    )
    e_prompt = jnp.exp(s_prompt - largest)
    e_cache = jnp.exp(s_cache - largest)
    e_tree = jnp.exp(s_tree - largest)
    totals = (
        jnp.sum(e_prompt, axis=-1, keepdims=True)
        + jnp.sum(e_cache, axis=-1, keepdims=True)
        + jnp.sum(e_tree, axis=-1, keepdims=True)
    )
    w_prompt = (e_prompt / totals).astype(jnp.bfloat16)
    w_cache = (e_cache / totals).astype(jnp.bfloat16)
    w_tree = (e_tree / totals).astype(jnp.bfloat16)
    result = jnp.einsum("rnhp,hep->rnhe", w_prompt, prompt_v, preferred_element_type=jnp.float32)
    result = result + jnp.einsum(
        "rnhc,rhec->rnhe", w_cache, cache_v, preferred_element_type=jnp.float32
    )
    result = result + jnp.einsum(
        "rnhm,rmhe->rnhe", w_tree, new_values, preferred_element_type=jnp.float32
    )
    return result.astype(jnp.bfloat16)


CHUNKS = 1


def gather_like_all_to_all(block, axis_name):
    count = lax.psum(1, axis_name)
    copies = jnp.broadcast_to(block[None], (count,) + block.shape)
    return lax.all_to_all(copies, axis_name, 0, 0, tiled=True)


def per_device(
    inputs,
    query_weight,
    key_weight,
    value_weight,
    adapter_down,
    adapter_up,
    prompt_keys,
    prompt_values,
    cache_keys,
    cache_values,
    cache_lengths,
    parents,
    out_weight,
):
    along_x = lax.psum(1, "gyx")
    along_z = lax.psum(1, "gyz")
    groups = lax.psum(1, "gx")
    node_count = parents.shape[1]
    head_width = query_weight.shape[0]
    head_count = head_width // HEAD
    per_x = groups // along_x
    columns = out_weight.shape[1]
    every_block = gather_like_all_to_all(out_weight, "gx")
    width = columns * groups // (along_x * along_z)
    every_block = every_block.reshape(along_x, per_x, head_width, columns // width, width)
    sent = every_block.transpose(1, 3, 0, 2, 4).reshape(along_z, along_x, head_width, width)
    own_block = lax.all_to_all(sent, "gyz", 0, 0, tiled=True)
    folded = jnp.dot(adapter_up, adapter_down, preferred_element_type=jnp.float32)
    folded = (query_weight.astype(jnp.float32) + folded).astype(jnp.bfloat16)
    weights = jnp.concatenate([folded, key_weight, value_weight], axis=0)
    local = inputs.shape[0]
    rows = local // CHUNKS
    results = []
    for chunk in range(CHUNKS):
        piece = inputs[chunk * rows : (chunk + 1) * rows]
        gathered = lax.all_gather(piece, GY, axis=0, tiled=True)
        if chunk == CHUNKS - 1:
            gathered, own_block, weights = lax.optimization_barrier((gathered, own_block, weights))
        mixture = lax.psum_scatter(
            contract_rows(gathered, weights),
            "gx",
            scatter_dimension=0,
            tiled=True,
        )
        queries = mixture[:, :head_width].astype(jnp.bfloat16)
        new_keys = mixture[:, head_width : 2 * head_width].astype(jnp.bfloat16)
        new_values = mixture[:, 2 * head_width :].astype(jnp.bfloat16)
        requests = mixture.shape[0] // node_count
        shaped = (requests, node_count, head_count, HEAD)
        cached = (requests, head_count, HEAD, cache_keys.shape[2])
        attended = attend(
            queries.reshape(shaped),
            new_keys.reshape(shaped),
            new_values.reshape(shaped),
            prompt_keys,
            prompt_values,
            cache_keys[chunk::CHUNKS].reshape(cached),
            cache_values[chunk::CHUNKS].reshape(cached),
            cache_lengths[chunk::CHUNKS],
            parents[chunk::CHUNKS],
        )
        flattened = attended.reshape(requests * node_count, head_width)
        heads_along_z = lax.all_gather(flattened, "gyz", axis=0)
        partial_sums = jnp.einsum(
            "zte,zxec->txc", heads_along_z, own_block, preferred_element_type=jnp.float32
        )
        pieces = partial_sums.astype(jnp.bfloat16)
        landed = lax.all_to_all(pieces, "gyx", 1, 1, tiled=True)
        out = jnp.sum(landed.astype(jnp.float32), axis=1).astype(jnp.bfloat16)
        results.append(out.reshape(requests, node_count, -1))
    stacked = jnp.stack(results, axis=1)
    return stacked.reshape(-1, stacked.shape[-1])


def split_mesh(mesh):
    devices = mesh.devices
    along_x = len({d.coords[0] for d in devices[0]})
    shape = (devices.shape[0], along_x, devices.shape[1] // along_x)
    return Mesh(devices.reshape(shape), ("gx",) + GY)


def solution(mesh):
    placed = (
        P(GY, "gx"),
        P(GY, "gx"),
        P(GY, "gx"),
        P(GY, "gx"),
        P(None, "gx"),
        P(GY, None),
        P("gx", GY, None),
        P("gx", GY, None),
        P("gx", GY, None),
        P("gx", GY, None),
        P("gx"),
        P("gx", None),
        P(GY, "gx"),
    )
    return jax.shard_map(
        per_device, mesh=split_mesh(mesh), in_specs=placed, out_specs=P("gx", GY), check_vma=False
    )
```
